512 devices in a mesh: dp: 32 (over z, core), cent: 16 (over y, x).
Axes of the slice: x: 4, y: 4, z: 16, core: 2. Of those that a mesh axis runs over, the one named last changes fastest.
Arguments:
- points: bfloat16 [131072, 1024], P(('dp', 'cent')), may hold values from -22 to 22, as said below
- block_list: int32 [4096, 3], P(('dp', 'cent')), may hold values from 0 to 15, all different within a row; in each aligned block of 8 rows (0 to 7, 8 to 15, ...) at most 2 rows name the same one
- list_count: int32 [4096], P(('dp', 'cent')), may hold values from 1 to 3
- centroids: bfloat16 [16, 1024, 1024], P('cent', 'dp'), may hold values from -14 to 14, as said below
Outputs:
- new_centroids: float32 [16, 1024, 1024], P('cent', 'dp')
The draws below stay inside these ranges and needn't reach their ends.
Inputs may be any that keep to these rules, and one draw needn't show every extreme that they name: `block_list`: within the rows of one device (aligned blocks of 8 rows) no block id appears more than 2 times, and the ids of one row differ. Only the first list_count[t] entries of row t of block_list are valid. `points`: Real-valued embeddings. Real-valued centroids.
All inputs are finite; a program needn't handle non-finite values.
Results may differ from the reference program's by a relative error of at most 0.0019.
Values may be sent and summed in bfloat16 or wider, within the bound.
No kernel may reach another device: no remote copies, remote signals or barrier semaphores. Data moves between devices by JAX's collectives and lax.ppermute only.
A program may use at most 64 MiB of HBM per device.

```python
import math
import jax
import jax.numpy as jnp
import numpy as np
from jax import lax

D = 1024
CB = 1024
NL = 3
TILE = 32
TPD = 8
NBLK = 16
CAP = 2
NTILES = 4096
NPTS = 131072
N_DP = 32
N_CENT = 16


def draw_centroids(key, part):
    inner = jax.random.fold_in(key, 23)
    values = jnp.clip(jax.random.normal(inner, (NBLK, CB, D), jnp.float32), -6.0, 6.0)
    return values.astype(jnp.bfloat16)


def draw_points(key, part):
    inner = jax.random.fold_in(key, 37)
    values = jnp.clip(jax.random.normal(inner, (NPTS, D), jnp.float32), -6.0, 6.0)
    return values.astype(jnp.bfloat16)


def touch_ends(result, rng, smallest, top_value):
    extent = result.shape
    index_at = [jax.random.randint(jax.random.fold_in(rng, axis), (), 0, extent[axis]) for axis in range(len(extent))]
    result = result.at[tuple(index_at)].set(smallest)
    longest = extent.index(max(extent))
    index_at[longest] = (index_at[longest] + 1) % extent[longest]
    return result.at[tuple(index_at)].set(top_value)


def routed_block(stream_key, own, number, rows, amount, top, bound, lean):
    order = jax.random.permutation(stream_key, amount)
    packed, usual = load_shares(amount, rows * top, bound, lean, True), load_shares(amount, rows * top, bound, lean, False)
    places = jnp.arange(amount)

    def named(lengths, rotation):
        used = int((lengths > 0).sum())
        fixed = max(1, used // 4)
        passed = fixed + (places - fixed + rotation * (used - fixed)) % max(1, amount - fixed)
        return jnp.zeros((amount,), jnp.int32).at[order[jnp.where(places < fixed, places, passed)]].set(jnp.asarray(lengths, jnp.int32))

    lengths = jnp.where(number % 4 == 0, named(packed, number // 4), named(usual, number - number // 4 - 1))
    mixed = jax.random.permutation(jax.random.fold_in(own, 3), amount)
    giver, sink = mixed[0:amount // 2 * 2:2], mixed[1:amount // 2 * 2:2]
    margin = jnp.minimum(lengths[giver] - 1, bound - lengths[sink]) // 2
    margin = jnp.where((giver == order[0]) | (sink == order[0]) | (lengths[sink] == 0), 0, jnp.maximum(margin, 0))
    passed = jax.random.randint(jax.random.fold_in(own, 4), (amount // 2,), 0, 1 << 20) % (margin + 1)
    lengths = lengths.at[giver].add(-passed).at[sink].add(passed)
    members = jnp.searchsorted(jnp.cumsum(lengths), jnp.arange(rows * top), side="right").astype(jnp.int32)
    table = members.reshape(top, rows).T
    table = table[jax.random.permutation(jax.random.fold_in(own, 1), rows)]
    rotation = jax.random.randint(jax.random.fold_in(own, 2), (rows, 1), 0, top)
    return jnp.take_along_axis(table, (jnp.arange(top)[None, :] + rotation) % top, axis=1)


def load_shares(count, total, limit, lean, full):
    portions = [(1 << 20) // math.isqrt(standing ** lean) + 1 for standing in range(1, count + 1)]
    largest = limit if full else min(limit, max(-(-total // count), total * portions[0] // sum(portions)))
    least = 1 if total - largest >= count - 1 else 0
    holding, spare = [largest] + [least] * (count - 1), total - largest - least * (count - 1)
    while spare > 0:
        free = [i for i in range(1, count) if holding[i] < largest] or [i for i in range(1, count) if holding[i] < limit]
        whole, remaining = sum([portions[i] for i in free]), spare
        for i in free:
            more = min(limit - holding[i], max(1, remaining * portions[i] // whole), spare)
            holding[i] = holding[i] + more
            spare = spare - more
    return np.array(holding)


def setup_inputs(seed: int = 0) -> dict:
    seeds = jax.random.split(jax.random.key(seed), 5)
    points = draw_points(jax.random.fold_in(seeds[4], 71), 0)
    block_list_keys = jax.random.split(jax.random.fold_in(seeds[1], 1), NTILES // TPD)
    block_list_turns = jax.random.permutation(jax.random.fold_in(seeds[1], 3), NTILES // TPD)
    block_list = jax.vmap(lambda own, number: routed_block(jax.random.fold_in(seeds[1], 2), own, number, TPD, NBLK, NL, CAP, 2))(block_list_keys, block_list_turns).reshape((NTILES, NL))
    list_count = touch_ends(jax.random.randint(seeds[2], (NTILES,), 1, NL + 1), jax.random.fold_in(seeds[2], 1), 1, NL).astype(jnp.int32)
    centroids = draw_centroids(jax.random.fold_in(seeds[4], 71), 0)
    return dict(points=points, block_list=block_list, list_count=list_count, centroids=centroids)


score_scale = 2.0
prior_weight = 1.0

def reference(points, block_list, list_count, centroids):
    group_tiles = N_CENT * TPD
    scale = score_scale / math.sqrt(D)
    tile_points = points.reshape(N_DP, group_tiles, TILE, D)
    group_lists = block_list.reshape(N_DP, group_tiles, NL)
    validity = jnp.arange(NL, dtype=jnp.int32)[None, :] < list_count[:, None]
    group_valid = validity.reshape(N_DP, group_tiles, NL)
    wide_centroids = centroids.astype(jnp.float32)

    def one_tile(carry, item):
        partial_sums, partial_mass = carry
        tile, block_ids, valid = item
        chosen = wide_centroids[block_ids]
        logits = jnp.einsum('pd,jkd->pjk', tile.astype(jnp.float32), chosen) * scale
        keep = valid[None, :, None]
        peak = lax.optimization_barrier(jnp.max(jnp.where(keep, logits, -1e+30), axis=(1, 2)))
        total = lax.optimization_barrier(jnp.sum(jnp.where(keep, jnp.exp(logits - peak[:, None, None]), 0.0), axis=(1, 2)))
        log_norm = peak + jnp.log(total)
        shares = jnp.where(keep, jnp.exp(logits - log_norm[:, None, None]), 0.0).astype(jnp.bfloat16)
        wide_shares = shares.astype(jnp.float32)
        weighted = jnp.einsum('pjk,pd->jkd', wide_shares, tile.astype(jnp.float32))
        partial_sums = partial_sums.at[block_ids].add(weighted)
        partial_mass = partial_mass.at[block_ids].add(lax.optimization_barrier(jnp.sum(wide_shares, axis=0)))
        return ((partial_sums, partial_mass), None)

    def one_group(carry, group):
        (group_sums, group_mass), unused = lax.scan(one_tile, carry, group)
        return ((group_sums, group_mass), None)
    start = (jnp.zeros((NBLK, CB, D), jnp.float32), jnp.zeros((NBLK, CB), jnp.float32))
    (sums, mass), unused = lax.scan(one_group, start, (tile_points, group_lists, group_valid))
    return (sums + prior_weight * wide_centroids) / (mass[:, :, None] + prior_weight)
```

```python
import math

import jax
import jax.numpy as jnp
from jax import lax
from jax.sharding import PartitionSpec as P

score_scale = 2.0
prior_weight = 1.0
empty_norm = 1e30


def combine_norms(peaks, totals, usable):
    keep = usable[..., None]
    highest = jnp.max(jnp.where(keep, peaks, -1e30), axis=-2)
    summed = jnp.sum(jnp.where(keep, totals * jnp.exp(peaks - highest[..., None, :]), 0.0), axis=-2)
    return highest + jnp.log(summed)


def per_device(points, block_list, list_count, centroids):
    owners = lax.axis_size("cent")
    tiles_here, listed = block_list.shape
    width = points.shape[1]
    tile_rows = points.shape[0] // tiles_here
    capacity = (tiles_here * listed + owners - 1) // owners
    slot_rows = capacity * tile_rows
    scale = score_scale / math.sqrt(width)
    usable = jnp.arange(listed, dtype=jnp.int32)[None, :] < list_count[:, None]
    naming = jnp.logical_and(
        block_list[:, :, None] == jnp.arange(owners, dtype=jnp.int32)[None, None, :],
        usable[:, :, None],
    )
    listing = jnp.any(naming, axis=1).astype(jnp.int32)
    earlier = jnp.cumsum(listing, axis=0) - listing
    placing = jnp.logical_and(
        listing.T[:, None, :] == 1,
        earlier.T[:, None, :] == jnp.arange(capacity, dtype=jnp.int32)[None, :, None],
    )
    placing = placing.astype(jnp.float32).reshape(owners * capacity, tiles_here)
    slot_rank = jnp.take_along_axis(earlier, block_list, axis=1)
    route_code = jnp.where(usable, block_list * capacity + slot_rank, -1)
    outgoing = jnp.dot(
        placing.astype(jnp.bfloat16),
        points.reshape(tiles_here, tile_rows * width),
        preferred_element_type=jnp.float32,
    )
    outgoing = outgoing.astype(jnp.bfloat16).reshape(owners, slot_rows, width)
    arrived = lax.all_to_all(outgoing, "cent", split_axis=0, concat_axis=0, tiled=True)
    incoming = arrived.reshape(owners * slot_rows, width)
    logits = (
        lax.dot_general(
            incoming,
            lax.all_gather(centroids, "dp", axis=1, tiled=True)[0],
            (((1,), (1,)), ((), ())),
            preferred_element_type=jnp.float32,
        )
        * scale
    )
    peaks = jnp.max(logits, axis=1)
    totals = jnp.sum(jnp.exp(logits - peaks[:, None]), axis=1)
    stats = jnp.stack(
        [peaks.reshape(owners, slot_rows), totals.reshape(owners, slot_rows)], axis=1
    )
    back = lax.all_to_all(stats, "cent", split_axis=0, concat_axis=0, tiled=True)
    back_peaks = back[:, 0].reshape(owners * capacity, tile_rows)
    back_totals = back[:, 1].reshape(owners * capacity, tile_rows)
    lookup = jnp.where(usable, route_code, 0)
    tile_norms = combine_norms(back_peaks[lookup], back_totals[lookup], usable)
    empty = 1.0 - jnp.sum(placing, axis=1)
    slot_norms = (
        jnp.dot(placing, tile_norms, precision=lax.Precision.HIGHEST)
        + empty[:, None] * empty_norm
    )
    row_norms = lax.all_to_all(
        slot_norms.reshape(owners, slot_rows), "cent", split_axis=0, concat_axis=0, tiled=True
    ).reshape(-1)
    shares = jnp.exp(logits - row_norms[:, None]).astype(jnp.bfloat16)
    own_rows = centroids[0].astype(jnp.float32)
    marker = (jnp.arange(128, dtype=jnp.int32) == 0).astype(jnp.bfloat16)
    widened = jnp.concatenate(
        [incoming, jnp.broadcast_to(marker[None, :], (incoming.shape[0], 128))], axis=1
    )
    block_sums = lax.dot_general(
        shares, widened, (((0,), (0,)), ((), ())), preferred_element_type=jnp.float32
    )
    reduced = lax.psum_scatter(block_sums, "dp", scatter_dimension=0, tiled=True)
    new_sums = reduced[:, :width]
    new_mass = reduced[:, width]
    fresh = (new_sums + prior_weight * own_rows) / (new_mass[:, None] + prior_weight)
    return fresh[None]


def solution(mesh):
    in_specs = (
        P(("dp", "cent"), None),
        P(("dp", "cent"), None),
        P(("dp", "cent")),
        P("cent", "dp", None),
    )
    out_specs = P("cent", "dp", None)
    return jax.shard_map(
        per_device, mesh=mesh, in_specs=in_specs, out_specs=out_specs, check_vma=False
    )
```

```python
import math

import jax
import jax.numpy as jnp
from jax import lax
from jax.sharding import Mesh, PartitionSpec as P

score_scale = 2.0
prior_weight = 1.0
empty_norm = 1e30


def combine_norms(peaks, totals, usable):
    keep = usable[..., None]
    highest = jnp.max(jnp.where(keep, peaks, -1e30), axis=-2)
    summed = jnp.sum(jnp.where(keep, totals * jnp.exp(peaks - highest[..., None, :]), 0.0), axis=-2)
    return highest + jnp.log(summed)


def per_device(points, block_list, list_count, centroids):
    owners = lax.axis_size("cent")
    tiles_here, listed = block_list.shape
    width = points.shape[1]
    tile_rows = points.shape[0] // tiles_here
    capacity = (tiles_here * listed + owners - 1) // owners
    slot_rows = capacity * tile_rows
    scale = score_scale / math.sqrt(width)
    usable = jnp.arange(listed, dtype=jnp.int32)[None, :] < list_count[:, None]
    naming = jnp.logical_and(
        block_list[:, :, None] == jnp.arange(owners, dtype=jnp.int32)[None, None, :],
        usable[:, :, None],
    )
    listing = jnp.any(naming, axis=1).astype(jnp.int32)
    earlier = jnp.cumsum(listing, axis=0) - listing
    placing = jnp.logical_and(
        listing.T[:, None, :] == 1,
        earlier.T[:, None, :] == jnp.arange(capacity, dtype=jnp.int32)[None, :, None],
    )
    placing = placing.astype(jnp.float32).reshape(owners * capacity, tiles_here)
    slot_rank = jnp.take_along_axis(earlier, block_list, axis=1)
    route_code = jnp.where(usable, block_list * capacity + slot_rank, -1)
    outgoing = jnp.dot(
        placing.astype(jnp.bfloat16),
        points.reshape(tiles_here, tile_rows * width),
        preferred_element_type=jnp.float32,
    )
    outgoing = outgoing.astype(jnp.bfloat16).reshape(owners, slot_rows, width)
    arrived = lax.all_to_all(outgoing, "cent", split_axis=0, concat_axis=0, tiled=True)
    incoming = arrived.reshape(owners * slot_rows, width)
    logits = (
        lax.dot_general(
            incoming,
            lax.all_gather(centroids, ("z", "core"), axis=1, tiled=True)[0],
            (((1,), (1,)), ((), ())),
            preferred_element_type=jnp.float32,
        )
        * scale
    )
    peaks = jnp.max(logits, axis=1)
    totals = jnp.sum(jnp.exp(logits - peaks[:, None]), axis=1)
    stats = jnp.stack(
        [peaks.reshape(owners, slot_rows), totals.reshape(owners, slot_rows)], axis=1
    )
    back = lax.all_to_all(stats, "cent", split_axis=0, concat_axis=0, tiled=True)
    back_peaks = back[:, 0].reshape(owners * capacity, tile_rows)
    back_totals = back[:, 1].reshape(owners * capacity, tile_rows)
    lookup = jnp.where(usable, route_code, 0)
    tile_norms = combine_norms(back_peaks[lookup], back_totals[lookup], usable)
    empty = 1.0 - jnp.sum(placing, axis=1)
    slot_norms = (
        jnp.dot(placing, tile_norms, precision=lax.Precision.HIGHEST)
        + empty[:, None] * empty_norm
    )
    row_norms = lax.all_to_all(
        slot_norms.reshape(owners, slot_rows), "cent", split_axis=0, concat_axis=0, tiled=True
    ).reshape(-1)
    shares = jnp.exp(logits - row_norms[:, None]).astype(jnp.bfloat16)
    own_rows = centroids[0].astype(jnp.float32)
    marker = (jnp.arange(128, dtype=jnp.int32) == 0).astype(jnp.bfloat16)
    widened = jnp.concatenate(
        [incoming, jnp.broadcast_to(marker[None, :], (incoming.shape[0], 128))], axis=1
    )
    block_sums = lax.dot_general(
        shares, widened, (((0,), (0,)), ((), ())), preferred_element_type=jnp.float32
    )
    n_core = lax.axis_size("core")
    core = lax.axis_index("core")
    by_owner = block_sums.reshape(lax.axis_size("z"), n_core, -1, block_sums.shape[1])
    mine = lax.dynamic_index_in_dim(by_owner, core, axis=1, keepdims=False)
    other = lax.dynamic_index_in_dim(by_owner, n_core - 1 - core, axis=1, keepdims=False)
    paired = mine + lax.ppermute(other, "core", [(0, 1), (1, 0)])
    reduced = lax.psum_scatter(paired, "z", scatter_dimension=0, tiled=True)[0]
    new_sums = reduced[:, :width]
    new_mass = reduced[:, width]
    fresh = (new_sums + prior_weight * own_rows) / (new_mass[:, None] + prior_weight)
    return fresh[None]


def solution(mesh):
    cores = 2
    split = Mesh(
        mesh.devices.reshape(mesh.shape["dp"] // cores, cores, mesh.shape["cent"]),
        ("z", "core", "cent"),
    )
    rows = ("z", "core")
    in_specs = (
        P((*rows, "cent"), None),
        P((*rows, "cent"), None),
        P((*rows, "cent")),
        P("cent", rows, None),
    )
    out_specs = P("cent", rows, None)
    return jax.shard_map(
        per_device, mesh=split, in_specs=in_specs, out_specs=out_specs, check_vma=False
    )
```

```python
import math

import jax
import jax.numpy as jnp
from jax import lax
from jax.sharding import Mesh, PartitionSpec as P

score_scale = 2.0
prior_weight = 1.0
empty_norm = 1e30


def combine_norms(peaks, totals, usable):
    keep = usable[..., None]
    highest = jnp.max(jnp.where(keep, peaks, -1e30), axis=-2)
    summed = jnp.sum(jnp.where(keep, totals * jnp.exp(peaks - highest[..., None, :]), 0.0), axis=-2)
    return highest + jnp.log(summed)


def per_device(points, block_list, list_count, centroids):
    owners = lax.axis_size("cent")
    tiles_here, listed = block_list.shape
    width = points.shape[1]
    tile_rows = points.shape[0] // tiles_here
    capacity = (tiles_here * listed + owners - 1) // owners
    slot_rows = capacity * tile_rows
    scale = score_scale / math.sqrt(width)
    usable = jnp.arange(listed, dtype=jnp.int32)[None, :] < list_count[:, None]
    naming = jnp.logical_and(
        block_list[:, :, None] == jnp.arange(owners, dtype=jnp.int32)[None, None, :],
        usable[:, :, None],
    )
    listing = jnp.any(naming, axis=1).astype(jnp.int32)
    earlier = jnp.cumsum(listing, axis=0) - listing
    placing = jnp.logical_and(
        listing.T[:, None, :] == 1,
        earlier.T[:, None, :] == jnp.arange(capacity, dtype=jnp.int32)[None, :, None],
    )
    placing = placing.astype(jnp.float32).reshape(owners * capacity, tiles_here)
    slot_rank = jnp.take_along_axis(earlier, block_list, axis=1)
    route_code = jnp.where(usable, block_list * capacity + slot_rank, -1)
    outgoing = jnp.dot(
        placing.astype(jnp.bfloat16),
        points.reshape(tiles_here, tile_rows * width),
        preferred_element_type=jnp.float32,
    )
    outgoing = outgoing.astype(jnp.bfloat16).reshape(owners, slot_rows, width)
    arrived = lax.all_to_all(outgoing, "cent", split_axis=0, concat_axis=0, tiled=True)
    incoming = arrived.reshape(owners * slot_rows, width)
    logits = (
        lax.dot_general(
            incoming,
            lax.all_gather(centroids, ("z", "core"), axis=1, tiled=True)[0],
            (((1,), (1,)), ((), ())),
            preferred_element_type=jnp.float32,
        )
        * scale
    )
    peaks = jnp.max(logits, axis=1)
    totals = jnp.sum(jnp.exp(logits - peaks[:, None]), axis=1)
    stats = jnp.stack(
        [peaks.reshape(owners, slot_rows), totals.reshape(owners, slot_rows)], axis=1
    )
    back = lax.all_to_all(stats, "cent", split_axis=0, concat_axis=0, tiled=True)
    back_peaks = back[:, 0].reshape(owners * capacity, tile_rows)
    back_totals = back[:, 1].reshape(owners * capacity, tile_rows)
    lookup = jnp.where(usable, route_code, 0)
    tile_norms = combine_norms(back_peaks[lookup], back_totals[lookup], usable)
    empty = 1.0 - jnp.sum(placing, axis=1)
    slot_norms = (
        jnp.dot(placing, tile_norms, precision=lax.Precision.HIGHEST)
        + empty[:, None] * empty_norm
    )
    row_norms = lax.all_to_all(
        slot_norms.reshape(owners, slot_rows), "cent", split_axis=0, concat_axis=0, tiled=True
    ).reshape(-1)
    shares = jnp.exp(logits - row_norms[:, None]).astype(jnp.bfloat16)
    own_rows = centroids[0].astype(jnp.float32)
    marker = (jnp.arange(128, dtype=jnp.int32) == 0).astype(jnp.bfloat16)
    widened = jnp.concatenate(
        [incoming, jnp.broadcast_to(marker[None, :], (incoming.shape[0], 128))], axis=1
    )
    n_core = lax.axis_size("core")
    core = lax.axis_index("core")
    by_owner = shares.reshape(shares.shape[0], lax.axis_size("z"), n_core, -1)

    def owner_sums(which):
        picked = lax.dynamic_index_in_dim(by_owner, which, axis=2, keepdims=False)
        return lax.dot_general(
            picked, widened, (((0,), (0,)), ((), ())), preferred_element_type=jnp.float32
        )

    sent = lax.ppermute(owner_sums(n_core - 1 - core), "core", [(0, 1), (1, 0)])
    paired = lax.optimization_barrier(owner_sums(core)) + sent
    reduced = lax.psum_scatter(paired, "z", scatter_dimension=0, tiled=True)[0]
    new_sums = reduced[:, :width]
    new_mass = reduced[:, width]
    fresh = (new_sums + prior_weight * own_rows) / (new_mass[:, None] + prior_weight)
    return fresh[None]


def solution(mesh):
    cores = 2
    split = Mesh(
        mesh.devices.reshape(mesh.shape["dp"] // cores, cores, mesh.shape["cent"]),
        ("z", "core", "cent"),
    )
    rows = ("z", "core")
    in_specs = (
        P((*rows, "cent"), None),
        P((*rows, "cent"), None),
        P((*rows, "cent")),
        P("cent", rows, None),
    )
    out_specs = P("cent", rows, None)
    return jax.shard_map(
        per_device, mesh=split, in_specs=in_specs, out_specs=out_specs, check_vma=False
    )
```

```python
import math

import jax
import jax.numpy as jnp
from jax import lax
from jax.sharding import Mesh, PartitionSpec as P

score_scale = 2.0
prior_weight = 1.0
empty_norm = 1e30


def combine_norms(peaks, totals, usable):
    keep = usable[..., None]
    highest = jnp.max(jnp.where(keep, peaks, -1e30), axis=-2)
    summed = jnp.sum(jnp.where(keep, totals * jnp.exp(peaks - highest[..., None, :]), 0.0), axis=-2)
    return highest + jnp.log(summed)


def per_device(points, block_list, list_count, centroids):
    owners = lax.axis_size("cent")
    tiles_here, listed = block_list.shape
    width = points.shape[1]
    tile_rows = points.shape[0] // tiles_here
    capacity = (tiles_here * listed + owners - 1) // owners
    slot_rows = capacity * tile_rows
    scale = score_scale / math.sqrt(width)
    usable = jnp.arange(listed, dtype=jnp.int32)[None, :] < list_count[:, None]
    naming = jnp.logical_and(
        block_list[:, :, None] == jnp.arange(owners, dtype=jnp.int32)[None, None, :],
        usable[:, :, None],
    )
    listing = jnp.any(naming, axis=1).astype(jnp.int32)
    earlier = jnp.cumsum(listing, axis=0) - listing
    placing = jnp.logical_and(
        listing.T[:, None, :] == 1,
        earlier.T[:, None, :] == jnp.arange(capacity, dtype=jnp.int32)[None, :, None],
    )
    placing = placing.astype(jnp.float32).reshape(owners * capacity, tiles_here)
    slot_rank = jnp.take_along_axis(earlier, block_list, axis=1)
    route_code = jnp.where(usable, block_list * capacity + slot_rank, -1)
    outgoing = jnp.dot(
        placing.astype(jnp.bfloat16),
        points.reshape(tiles_here, tile_rows * width),
        preferred_element_type=jnp.float32,
    )
    outgoing = outgoing.astype(jnp.bfloat16).reshape(owners, slot_rows, width)
    slot_routes = (
        jnp.dot(placing, (route_code + 1).astype(jnp.float32), precision=lax.Precision.HIGHEST)
        - 1.0
    )
    slot_routes = jnp.round(slot_routes).astype(jnp.int32).reshape(owners, capacity, listed)
    arrived = lax.all_to_all(outgoing, "cent", split_axis=0, concat_axis=0, tiled=True)
    arrived_routes = lax.all_to_all(slot_routes, "cent", split_axis=0, concat_axis=0, tiled=True)
    incoming = arrived.reshape(owners * slot_rows, width)
    logits = (
        lax.dot_general(
            incoming,
            lax.all_gather(centroids, ("z", "core"), axis=1, tiled=True)[0],
            (((1,), (1,)), ((), ())),
            preferred_element_type=jnp.float32,
        )
        * scale
    )
    peaks = jnp.max(logits, axis=1)
    totals = jnp.sum(jnp.exp(logits - peaks[:, None]), axis=1)
    every = lax.all_gather(jnp.stack([peaks, totals]), "cent", axis=0, tiled=False)
    every = every.reshape(owners, 2, owners, capacity, tile_rows)
    held = arrived_routes >= 0
    code = jnp.maximum(arrived_routes, 0)
    source = jnp.arange(owners, dtype=jnp.int32)[:, None, None]
    slot_norms = combine_norms(
        every[code // capacity, 0, source, code % capacity],
        every[code // capacity, 1, source, code % capacity],
        held,
    )
    row_norms = jnp.where(jnp.any(held, axis=-1)[..., None], slot_norms, empty_norm).reshape(-1)
    shares = jnp.exp(logits - row_norms[:, None]).astype(jnp.bfloat16)
    own_rows = centroids[0].astype(jnp.float32)
    marker = (jnp.arange(128, dtype=jnp.int32) == 0).astype(jnp.bfloat16)
    widened = jnp.concatenate(
        [incoming, jnp.broadcast_to(marker[None, :], (incoming.shape[0], 128))], axis=1
    )
    n_core = lax.axis_size("core")
    core = lax.axis_index("core")
    by_owner = shares.reshape(shares.shape[0], lax.axis_size("z"), n_core, -1)

    def owner_sums(which):
        picked = lax.dynamic_index_in_dim(by_owner, which, axis=2, keepdims=False)
        return lax.dot_general(
            picked, widened, (((0,), (0,)), ((), ())), preferred_element_type=jnp.float32
        )

    sent = lax.ppermute(owner_sums(n_core - 1 - core), "core", [(0, 1), (1, 0)])
    paired = lax.optimization_barrier(owner_sums(core)) + sent
    reduced = lax.psum_scatter(paired, "z", scatter_dimension=0, tiled=True)[0]
    new_sums = reduced[:, :width]
    new_mass = reduced[:, width]
    fresh = (new_sums + prior_weight * own_rows) / (new_mass[:, None] + prior_weight)
    return fresh[None]


def solution(mesh):
    cores = 2
    split = Mesh(
        mesh.devices.reshape(mesh.shape["dp"] // cores, cores, mesh.shape["cent"]),
        ("z", "core", "cent"),
    )
    rows = ("z", "core")
    in_specs = (
        P((*rows, "cent"), None),
        P((*rows, "cent"), None),
        P((*rows, "cent")),
        P("cent", rows, None),
    )
    out_specs = P("cent", rows, None)
    return jax.shard_map(
        per_device, mesh=split, in_specs=in_specs, out_specs=out_specs, check_vma=False
    )
```

```python
import math

import jax
import jax.numpy as jnp
from jax import lax
from jax.sharding import Mesh, PartitionSpec as P

score_scale = 2.0
prior_weight = 1.0
empty_norm = 1e30


def combine_norms(peaks, totals, usable):
    keep = usable[..., None]
    highest = jnp.max(jnp.where(keep, peaks, -1e30), axis=-2)
    summed = jnp.sum(jnp.where(keep, totals * jnp.exp(peaks - highest[..., None, :]), 0.0), axis=-2)
    return highest + jnp.log(summed)


def per_device(points, block_list, list_count, centroids):
    owners = lax.axis_size("cent")
    tiles_here, listed = block_list.shape
    width = points.shape[1]
    tile_rows = points.shape[0] // tiles_here
    capacity = (tiles_here * listed + owners - 1) // owners
    slot_rows = capacity * tile_rows
    scale = score_scale / math.sqrt(width)
    usable = jnp.arange(listed, dtype=jnp.int32)[None, :] < list_count[:, None]
    naming = jnp.logical_and(
        block_list[:, :, None] == jnp.arange(owners, dtype=jnp.int32)[None, None, :],
        usable[:, :, None],
    )
    listing = jnp.any(naming, axis=1).astype(jnp.int32)
    earlier = jnp.cumsum(listing, axis=0) - listing
    placing = jnp.logical_and(
        listing.T[:, None, :] == 1,
        earlier.T[:, None, :] == jnp.arange(capacity, dtype=jnp.int32)[None, :, None],
    )
    placing = placing.astype(jnp.float32).reshape(owners * capacity, tiles_here)
    slot_rank = jnp.take_along_axis(earlier, block_list, axis=1)
    route_code = jnp.where(usable, block_list * capacity + slot_rank, -1)
    outgoing = jnp.dot(
        placing.astype(jnp.bfloat16),
        points.reshape(tiles_here, tile_rows * width),
        preferred_element_type=jnp.float32,
    )
    outgoing = outgoing.astype(jnp.bfloat16).reshape(owners, slot_rows, width)
    slot_routes = (
        jnp.dot(placing, (route_code + 1).astype(jnp.float32), precision=lax.Precision.HIGHEST)
        - 1.0
    )
    slot_routes = jnp.round(slot_routes).astype(jnp.int32).reshape(owners, capacity, listed)
    arrived = lax.all_to_all(outgoing, "cent", split_axis=0, concat_axis=0, tiled=True)
    arrived_routes = lax.all_to_all(slot_routes, "cent", split_axis=0, concat_axis=0, tiled=True)
    incoming = arrived.reshape(owners * slot_rows, width)
    logits = (
        lax.dot_general(
            incoming,
            lax.all_gather(centroids, ("z", "core"), axis=1, tiled=True)[0],
            (((1,), (1,)), ((), ())),
            preferred_element_type=jnp.float32,
        )
        * scale
    )
    peaks = jnp.max(logits, axis=1)
    totals = jnp.sum(jnp.exp(logits - peaks[:, None]), axis=1)
    stats = jnp.stack([peaks, totals])
    every = lax.all_to_all(
        jnp.broadcast_to(stats[None], (owners, *stats.shape)),
        "cent",
        split_axis=0,
        concat_axis=0,
        tiled=True,
    )
    every = every.reshape(owners, 2, owners, capacity, tile_rows)
    held = arrived_routes >= 0
    code = jnp.maximum(arrived_routes, 0)
    source = jnp.arange(owners, dtype=jnp.int32)[:, None, None]
    slot_norms = combine_norms(
        every[code // capacity, 0, source, code % capacity],
        every[code // capacity, 1, source, code % capacity],
        held,
    )
    row_norms = jnp.where(jnp.any(held, axis=-1)[..., None], slot_norms, empty_norm).reshape(-1)
    shares = jnp.exp(logits - row_norms[:, None]).astype(jnp.bfloat16)
    own_rows = centroids[0].astype(jnp.float32)
    marker = (jnp.arange(128, dtype=jnp.int32) == 0).astype(jnp.bfloat16)
    widened = jnp.concatenate(
        [incoming, jnp.broadcast_to(marker[None, :], (incoming.shape[0], 128))], axis=1
    )
    n_core = lax.axis_size("core")
    core = lax.axis_index("core")
    by_owner = shares.reshape(shares.shape[0], lax.axis_size("z"), n_core, -1)

    def owner_sums(which):
        picked = lax.dynamic_index_in_dim(by_owner, which, axis=2, keepdims=False)
        return lax.dot_general(
            picked, widened, (((0,), (0,)), ((), ())), preferred_element_type=jnp.float32
        )

    sent = lax.ppermute(owner_sums(n_core - 1 - core), "core", [(0, 1), (1, 0)])
    paired = lax.optimization_barrier(owner_sums(core)) + sent
    reduced = lax.psum_scatter(paired, "z", scatter_dimension=0, tiled=True)[0]
    new_sums = reduced[:, :width]
    new_mass = reduced[:, width]
    fresh = (new_sums + prior_weight * own_rows) / (new_mass[:, None] + prior_weight)
    return fresh[None]


def solution(mesh):
    cores = 2
    split = Mesh(
        mesh.devices.reshape(mesh.shape["dp"] // cores, cores, mesh.shape["cent"]),
        ("z", "core", "cent"),
    )
    rows = ("z", "core")
    in_specs = (
        P((*rows, "cent"), None),
        P((*rows, "cent"), None),
        P((*rows, "cent")),
        P("cent", rows, None),
    )
    out_specs = P("cent", rows, None)
    return jax.shard_map(
        per_device, mesh=split, in_specs=in_specs, out_specs=out_specs, check_vma=False
    )
```

```python
import math

import jax
import jax.numpy as jnp
from jax import lax
from jax.sharding import Mesh, PartitionSpec as P

score_scale = 2.0
prior_weight = 1.0
empty_norm = 1e30


def combine_norms(peaks, totals, usable):
    keep = usable[..., None]
    highest = jnp.max(jnp.where(keep, peaks, -1e30), axis=-2)
    summed = jnp.sum(jnp.where(keep, totals * jnp.exp(peaks - highest[..., None, :]), 0.0), axis=-2)
    return highest + jnp.log(summed)


def gather_block(rows_here):
    core = lax.axis_index("core")
    high = lax.all_gather(rows_here, "zh", axis=0, tiled=True)
    mine = lax.all_gather(high, "zl", axis=0, tiled=True)
    other = lax.ppermute(mine, "core", [(0, 1), (1, 0)])
    first = jnp.where(core == 0, mine, other)
    second = jnp.where(core == 0, other, mine)
    shape = (lax.axis_size("zl"), lax.axis_size("zh"), *rows_here.shape)
    both = jnp.stack([first.reshape(shape), second.reshape(shape)], axis=2)
    return both.transpose(1, 0, 2, 3, 4).reshape(-1, rows_here.shape[-1])


def per_device(points, block_list, list_count, centroids):
    owners = lax.axis_size("cent")
    tiles_here, listed = block_list.shape
    width = points.shape[1]
    tile_rows = points.shape[0] // tiles_here
    capacity = (tiles_here * listed + owners - 1) // owners
    slot_rows = capacity * tile_rows
    scale = score_scale / math.sqrt(width)
    usable = jnp.arange(listed, dtype=jnp.int32)[None, :] < list_count[:, None]
    naming = jnp.logical_and(
        block_list[:, :, None] == jnp.arange(owners, dtype=jnp.int32)[None, None, :],
        usable[:, :, None],
    )
    listing = jnp.any(naming, axis=1).astype(jnp.int32)
    earlier = jnp.cumsum(listing, axis=0) - listing
    placing = jnp.logical_and(
        listing.T[:, None, :] == 1,
        earlier.T[:, None, :] == jnp.arange(capacity, dtype=jnp.int32)[None, :, None],
    )
    placing = placing.astype(jnp.float32).reshape(owners * capacity, tiles_here)
    slot_rank = jnp.take_along_axis(earlier, block_list, axis=1)
    route_code = jnp.where(usable, block_list * capacity + slot_rank, -1)
    outgoing = jnp.dot(
        placing.astype(jnp.bfloat16),
        points.reshape(tiles_here, tile_rows * width),
        preferred_element_type=jnp.float32,
    )
    outgoing = outgoing.astype(jnp.bfloat16).reshape(owners, slot_rows, width)
    slot_routes = (
        jnp.dot(placing, (route_code + 1).astype(jnp.float32), precision=lax.Precision.HIGHEST)
        - 1.0
    )
    slot_routes = jnp.round(slot_routes).astype(jnp.int32).reshape(owners, capacity, listed)
    arrived = lax.all_to_all(outgoing, "cent", split_axis=0, concat_axis=0, tiled=True)
    arrived_routes = lax.all_to_all(slot_routes, "cent", split_axis=0, concat_axis=0, tiled=True)
    incoming = arrived.reshape(owners * slot_rows, width)
    logits = (
        lax.dot_general(
            incoming,
            gather_block(centroids[0]),
            (((1,), (1,)), ((), ())),
            preferred_element_type=jnp.float32,
        )
        * scale
    )
    peaks = jnp.max(logits, axis=1)
    totals = jnp.sum(jnp.exp(logits - peaks[:, None]), axis=1)
    stats = jnp.stack([peaks, totals])
    every = lax.all_to_all(
        jnp.broadcast_to(stats[None], (owners, *stats.shape)),
        "cent",
        split_axis=0,
        concat_axis=0,
        tiled=True,
    )
    every = every.reshape(owners, 2, owners, capacity, tile_rows)
    held = arrived_routes >= 0
    code = jnp.maximum(arrived_routes, 0)
    source = jnp.arange(owners, dtype=jnp.int32)[:, None, None]
    slot_norms = combine_norms(
        every[code // capacity, 0, source, code % capacity],
        every[code // capacity, 1, source, code % capacity],
        held,
    )
    row_norms = jnp.where(jnp.any(held, axis=-1)[..., None], slot_norms, empty_norm).reshape(-1)
    shares = jnp.exp(logits - row_norms[:, None]).astype(jnp.bfloat16)
    own_rows = centroids[0].astype(jnp.float32)
    marker = (jnp.arange(128, dtype=jnp.int32) == 0).astype(jnp.bfloat16)
    widened = jnp.concatenate(
        [incoming, jnp.broadcast_to(marker[None, :], (incoming.shape[0], 128))], axis=1
    )
    n_core = lax.axis_size("core")
    core = lax.axis_index("core")
    n_z = lax.axis_size("zh") * lax.axis_size("zl")
    by_owner = shares.reshape(shares.shape[0], n_z, n_core, -1)

    def owner_sums(which):
        picked = lax.dynamic_index_in_dim(by_owner, which, axis=2, keepdims=False)
        return lax.dot_general(
            picked, widened, (((0,), (0,)), ((), ())), preferred_element_type=jnp.float32
        )

    sent = lax.ppermute(owner_sums(n_core - 1 - core), "core", [(0, 1), (1, 0)])
    paired = lax.optimization_barrier(owner_sums(core)) + sent
    reduced = lax.psum_scatter(paired, ("zh", "zl"), scatter_dimension=0, tiled=True)[0]
    new_sums = reduced[:, :width]
    new_mass = reduced[:, width]
    fresh = (new_sums + prior_weight * own_rows) / (new_mass[:, None] + prior_weight)
    return fresh[None]


def solution(mesh):
    cores = 2
    low = 4
    high = mesh.shape["dp"] // cores // low
    split = Mesh(
        mesh.devices.reshape(high, low, cores, mesh.shape["cent"]),
        ("zh", "zl", "core", "cent"),
    )
    rows = ("zh", "zl", "core")
    in_specs = (
        P((*rows, "cent"), None),
        P((*rows, "cent"), None),
        P((*rows, "cent")),
        P("cent", rows, None),
    )
    out_specs = P("cent", rows, None)
    return jax.shard_map(
        per_device, mesh=split, in_specs=in_specs, out_specs=out_specs, check_vma=False
    )
```

```python
import math

import jax
import jax.numpy as jnp
from jax import lax
from jax.sharding import Mesh, PartitionSpec as P

score_scale = 2.0
prior_weight = 1.0
empty_norm = 1e30


def combine_norms(peaks, totals, usable):
    keep = usable[..., None]
    highest = jnp.max(jnp.where(keep, peaks, -1e30), axis=-2)
    summed = jnp.sum(jnp.where(keep, totals * jnp.exp(peaks - highest[..., None, :]), 0.0), axis=-2)
    return highest + jnp.log(summed)


def gather_block(rows_here):
    core = lax.axis_index("core")
    spread = jnp.broadcast_to(rows_here[None], (lax.axis_size("zh"), *rows_here.shape))
    high = lax.all_to_all(spread, "zh", split_axis=0, concat_axis=0, tiled=True)
    high = high.reshape(-1, rows_here.shape[-1])
    mine = lax.all_gather(high, "zl", axis=0, tiled=True)
    other = lax.ppermute(mine, "core", [(0, 1), (1, 0)])
    first = jnp.where(core == 0, mine, other)
    second = jnp.where(core == 0, other, mine)
    shape = (lax.axis_size("zl"), lax.axis_size("zh"), *rows_here.shape)
    both = jnp.stack([first.reshape(shape), second.reshape(shape)], axis=2)
    return both.transpose(1, 0, 2, 3, 4).reshape(-1, rows_here.shape[-1])


def per_device(points, block_list, list_count, centroids):
    owners = lax.axis_size("cent")
    tiles_here, listed = block_list.shape
    width = points.shape[1]
    tile_rows = points.shape[0] // tiles_here
    capacity = (tiles_here * listed + owners - 1) // owners
    slot_rows = capacity * tile_rows
    scale = score_scale / math.sqrt(width)
    usable = jnp.arange(listed, dtype=jnp.int32)[None, :] < list_count[:, None]
    naming = jnp.logical_and(
        block_list[:, :, None] == jnp.arange(owners, dtype=jnp.int32)[None, None, :],
        usable[:, :, None],
    )
    listing = jnp.any(naming, axis=1).astype(jnp.int32)
    earlier = jnp.cumsum(listing, axis=0) - listing
    placing = jnp.logical_and(
        listing.T[:, None, :] == 1,
        earlier.T[:, None, :] == jnp.arange(capacity, dtype=jnp.int32)[None, :, None],
    )
    placing = placing.astype(jnp.float32).reshape(owners * capacity, tiles_here)
    slot_rank = jnp.take_along_axis(earlier, block_list, axis=1)
    route_code = jnp.where(usable, block_list * capacity + slot_rank, -1)
    outgoing = jnp.dot(
        placing.astype(jnp.bfloat16),
        points.reshape(tiles_here, tile_rows * width),
        preferred_element_type=jnp.float32,
    )
    outgoing = outgoing.astype(jnp.bfloat16).reshape(owners, slot_rows, width)
    slot_routes = (
        jnp.dot(placing, (route_code + 1).astype(jnp.float32), precision=lax.Precision.HIGHEST)
        - 1.0
    )
    slot_routes = jnp.round(slot_routes).astype(jnp.int32).reshape(owners, capacity, listed)
    arrived = lax.all_to_all(outgoing, "cent", split_axis=0, concat_axis=0, tiled=True)
    arrived_routes = lax.all_to_all(slot_routes, "cent", split_axis=0, concat_axis=0, tiled=True)
    incoming = arrived.reshape(owners * slot_rows, width)
    logits = (
        lax.dot_general(
            incoming,
            gather_block(centroids[0]),
            (((1,), (1,)), ((), ())),
            preferred_element_type=jnp.float32,
        )
        * scale
    )
    peaks = jnp.max(logits, axis=1)
    totals = jnp.sum(jnp.exp(logits - peaks[:, None]), axis=1)
    stats = jnp.stack([peaks, totals])
    every = lax.all_to_all(
        jnp.broadcast_to(stats[None], (owners, *stats.shape)),
        "cent",
        split_axis=0,
        concat_axis=0,
        tiled=True,
    )
    every = every.reshape(owners, 2, owners, capacity, tile_rows)
    held = arrived_routes >= 0
    code = jnp.maximum(arrived_routes, 0)
    source = jnp.arange(owners, dtype=jnp.int32)[:, None, None]
    slot_norms = combine_norms(
        every[code // capacity, 0, source, code % capacity],
        every[code // capacity, 1, source, code % capacity],
        held,
    )
    row_norms = jnp.where(jnp.any(held, axis=-1)[..., None], slot_norms, empty_norm).reshape(-1)
    shares = jnp.exp(logits - row_norms[:, None]).astype(jnp.bfloat16)
    own_rows = centroids[0].astype(jnp.float32)
    marker = (jnp.arange(128, dtype=jnp.int32) == 0).astype(jnp.bfloat16)
    widened = jnp.concatenate(
        [incoming, jnp.broadcast_to(marker[None, :], (incoming.shape[0], 128))], axis=1
    )
    n_core = lax.axis_size("core")
    core = lax.axis_index("core")
    n_z = lax.axis_size("zh") * lax.axis_size("zl")
    by_owner = shares.reshape(shares.shape[0], n_z, n_core, -1)

    def owner_sums(which):
        picked = lax.dynamic_index_in_dim(by_owner, which, axis=2, keepdims=False)
        return lax.dot_general(
            picked, widened, (((0,), (0,)), ((), ())), preferred_element_type=jnp.float32
        )

    sent = lax.ppermute(owner_sums(n_core - 1 - core), "core", [(0, 1), (1, 0)])
    paired = lax.optimization_barrier(owner_sums(core)) + sent
    reduced = lax.psum_scatter(paired, ("zh", "zl"), scatter_dimension=0, tiled=True)[0]
    new_sums = reduced[:, :width]
    new_mass = reduced[:, width]
    fresh = (new_sums + prior_weight * own_rows) / (new_mass[:, None] + prior_weight)
    return fresh[None]


def solution(mesh):
    cores = 2
    low = 4
    high = mesh.shape["dp"] // cores // low
    split = Mesh(
        mesh.devices.reshape(high, low, cores, mesh.shape["cent"]),
        ("zh", "zl", "core", "cent"),
    )
    rows = ("zh", "zl", "core")
    in_specs = (
        P((*rows, "cent"), None),
        P((*rows, "cent"), None),
        P((*rows, "cent")),
        P("cent", rows, None),
    )
    out_specs = P("cent", rows, None)
    return jax.shard_map(
        per_device, mesh=split, in_specs=in_specs, out_specs=out_specs, check_vma=False
    )
```

```python
import math

import jax
import jax.numpy as jnp
from jax import lax
from jax.sharding import Mesh, PartitionSpec as P

score_scale = 2.0
prior_weight = 1.0
empty_norm = 1e30


def combine_norms(peaks, totals, usable):
    keep = usable[..., None]
    highest = jnp.max(jnp.where(keep, peaks, -1e30), axis=-2)
    summed = jnp.sum(jnp.where(keep, totals * jnp.exp(peaks - highest[..., None, :]), 0.0), axis=-2)
    return highest + jnp.log(summed)


def gather_block(rows_here):
    core = lax.axis_index("core")
    high = lax.all_gather(rows_here, "zh", axis=0, tiled=True)
    mine = lax.all_gather(high, "zl", axis=0, tiled=True)
    other = lax.ppermute(mine, "core", [(0, 1), (1, 0)])
    first = jnp.where(core == 0, mine, other)
    second = jnp.where(core == 0, other, mine)
    shape = (lax.axis_size("zl"), lax.axis_size("zh"), *rows_here.shape)
    both = jnp.stack([first.reshape(shape), second.reshape(shape)], axis=2)
    return both.transpose(1, 0, 2, 3, 4).reshape(-1, rows_here.shape[-1])


def per_device(points, block_list, list_count, centroids):
    owners = lax.axis_size("cent")
    tiles_here, listed = block_list.shape
    width = points.shape[1]
    tile_rows = points.shape[0] // tiles_here
    capacity = (tiles_here * listed + owners - 1) // owners
    slot_rows = capacity * tile_rows
    scale = score_scale / math.sqrt(width)
    usable = jnp.arange(listed, dtype=jnp.int32)[None, :] < list_count[:, None]
    naming = jnp.logical_and(
        block_list[:, :, None] == jnp.arange(owners, dtype=jnp.int32)[None, None, :],
        usable[:, :, None],
    )
    listing = jnp.any(naming, axis=1).astype(jnp.int32)
    earlier = jnp.cumsum(listing, axis=0) - listing
    placing = jnp.logical_and(
        listing.T[:, None, :] == 1,
        earlier.T[:, None, :] == jnp.arange(capacity, dtype=jnp.int32)[None, :, None],
    )
    placing = placing.astype(jnp.float32).reshape(owners * capacity, tiles_here)
    slot_rank = jnp.take_along_axis(earlier, block_list, axis=1)
    route_code = jnp.where(usable, block_list * capacity + slot_rank, -1)
    outgoing = jnp.dot(
        placing.astype(jnp.bfloat16),
        points.reshape(tiles_here, tile_rows * width),
        preferred_element_type=jnp.float32,
    )
    outgoing = outgoing.astype(jnp.bfloat16).reshape(owners, slot_rows, width)
    slot_routes = (
        jnp.dot(placing, (route_code + 1).astype(jnp.float32), precision=lax.Precision.HIGHEST)
        - 1.0
    )
    slot_routes = jnp.round(slot_routes).astype(jnp.int32).reshape(owners, capacity, listed)
    arrived = lax.all_to_all(outgoing, "cent", split_axis=0, concat_axis=0, tiled=True)
    arrived_routes = lax.all_to_all(slot_routes, "cent", split_axis=0, concat_axis=0, tiled=True)
    incoming = arrived.reshape(owners * slot_rows, width)
    logits = (
        lax.dot_general(
            incoming,
            gather_block(centroids[0]),
            (((1,), (1,)), ((), ())),
            preferred_element_type=jnp.float32,
        )
        * scale
    )
    peaks = jnp.max(logits, axis=1)
    totals = jnp.sum(jnp.exp(logits - peaks[:, None]), axis=1)
    stats = jnp.stack([peaks, totals])
    every = lax.all_to_all(
        jnp.broadcast_to(stats[None], (owners, *stats.shape)),
        "cent",
        split_axis=0,
        concat_axis=0,
        tiled=True,
    )
    every = every.reshape(owners, 2, owners, capacity, tile_rows)
    held = arrived_routes >= 0
    code = jnp.maximum(arrived_routes, 0)
    source = jnp.arange(owners, dtype=jnp.int32)[:, None, None]
    picked = every[code // capacity, :, source, code % capacity]
    slot_norms = combine_norms(picked[..., 0, :], picked[..., 1, :], held)
    row_norms = jnp.where(jnp.any(held, axis=-1)[..., None], slot_norms, empty_norm).reshape(-1)
    shares = jnp.exp(logits - row_norms[:, None]).astype(jnp.bfloat16)
    own_rows = centroids[0].astype(jnp.float32)
    marker = (jnp.arange(128, dtype=jnp.int32) == 0).astype(jnp.bfloat16)
    widened = jnp.concatenate(
        [incoming, jnp.broadcast_to(marker[None, :], (incoming.shape[0], 128))], axis=1
    )
    n_core = lax.axis_size("core")
    core = lax.axis_index("core")
    n_z = lax.axis_size("zh") * lax.axis_size("zl")
    by_owner = shares.reshape(shares.shape[0], n_z, n_core, -1)

    def owner_sums(which):
        picked = lax.dynamic_index_in_dim(by_owner, which, axis=2, keepdims=False)
        return lax.dot_general(
            picked, widened, (((0,), (0,)), ((), ())), preferred_element_type=jnp.float32
        )

    sent = lax.ppermute(owner_sums(n_core - 1 - core), "core", [(0, 1), (1, 0)])
    paired = lax.optimization_barrier(owner_sums(core)) + sent
    reduced = lax.psum_scatter(paired, ("zh", "zl"), scatter_dimension=0, tiled=True)[0]
    new_sums = reduced[:, :width]
    new_mass = reduced[:, width]
    fresh = (new_sums + prior_weight * own_rows) / (new_mass[:, None] + prior_weight)
    return fresh[None]


def solution(mesh):
    cores = 2
    low = 4
    high = mesh.shape["dp"] // cores // low
    split = Mesh(
        mesh.devices.reshape(high, low, cores, mesh.shape["cent"]),
        ("zh", "zl", "core", "cent"),
    )
    rows = ("zh", "zl", "core")
    in_specs = (
        P((*rows, "cent"), None),
        P((*rows, "cent"), None),
        P((*rows, "cent")),
        P("cent", rows, None),
    )
    out_specs = P("cent", rows, None)
    return jax.shard_map(
        per_device, mesh=split, in_specs=in_specs, out_specs=out_specs, check_vma=False
    )
```

```python
import math

import jax
import jax.numpy as jnp
from jax import lax
from jax.sharding import Mesh, PartitionSpec as P

score_scale = 2.0
prior_weight = 1.0
empty_norm = 1e30


def combine_norms(peaks, totals, usable):
    keep = usable[..., None]
    highest = jnp.max(jnp.where(keep, peaks, -1e30), axis=-2)
    summed = jnp.sum(jnp.where(keep, totals * jnp.exp(peaks - highest[..., None, :]), 0.0), axis=-2)
    return highest + jnp.log(summed)


def gather_block(rows_here):
    high = lax.all_gather(rows_here, "zh", axis=0, tiled=True)
    mine = lax.all_gather(high, "zl", axis=0, tiled=True)
    other = lax.ppermute(mine, "core", [(0, 1), (1, 0)])
    return jnp.concatenate([mine, other], axis=0)


def per_device(points, block_list, list_count, centroids):
    owners = lax.axis_size("cent")
    tiles_here, listed = block_list.shape
    width = points.shape[1]
    tile_rows = points.shape[0] // tiles_here
    capacity = (tiles_here * listed + owners - 1) // owners
    slot_rows = capacity * tile_rows
    scale = score_scale / math.sqrt(width)
    usable = jnp.arange(listed, dtype=jnp.int32)[None, :] < list_count[:, None]
    naming = jnp.logical_and(
        block_list[:, :, None] == jnp.arange(owners, dtype=jnp.int32)[None, None, :],
        usable[:, :, None],
    )
    listing = jnp.any(naming, axis=1).astype(jnp.int32)
    earlier = jnp.cumsum(listing, axis=0) - listing
    placing = jnp.logical_and(
        listing.T[:, None, :] == 1,
        earlier.T[:, None, :] == jnp.arange(capacity, dtype=jnp.int32)[None, :, None],
    )
    placing = placing.astype(jnp.float32).reshape(owners * capacity, tiles_here)
    slot_rank = jnp.take_along_axis(earlier, block_list, axis=1)
    route_code = jnp.where(usable, block_list * capacity + slot_rank, -1)
    outgoing = jnp.dot(
        placing.astype(jnp.bfloat16),
        points.reshape(tiles_here, tile_rows * width),
        preferred_element_type=jnp.float32,
    )
    outgoing = outgoing.astype(jnp.bfloat16).reshape(owners, slot_rows, width)
    slot_routes = (
        jnp.dot(placing, (route_code + 1).astype(jnp.float32), precision=lax.Precision.HIGHEST)
        - 1.0
    )
    slot_routes = jnp.round(slot_routes).astype(jnp.int32).reshape(owners, capacity, listed)
    arrived = lax.all_to_all(outgoing, "cent", split_axis=0, concat_axis=0, tiled=True)
    arrived_routes = lax.all_to_all(slot_routes, "cent", split_axis=0, concat_axis=0, tiled=True)
    incoming = arrived.reshape(owners * slot_rows, width)
    logits = (
        lax.dot_general(
            incoming,
            gather_block(centroids[0]),
            (((1,), (1,)), ((), ())),
            preferred_element_type=jnp.float32,
        )
        * scale
    )
    peaks = jnp.max(logits, axis=1)
    totals = jnp.sum(jnp.exp(logits - peaks[:, None]), axis=1)
    stats = jnp.stack([peaks, totals])
    every = lax.all_to_all(
        jnp.broadcast_to(stats[None], (owners, *stats.shape)),
        "cent",
        split_axis=0,
        concat_axis=0,
        tiled=True,
    )
    every = every.reshape(owners, 2, owners, capacity, tile_rows)
    held = arrived_routes >= 0
    code = jnp.maximum(arrived_routes, 0)
    source = jnp.arange(owners, dtype=jnp.int32)[:, None, None]
    picked = every[code // capacity, :, source, code % capacity]
    slot_norms = combine_norms(picked[..., 0, :], picked[..., 1, :], held)
    row_norms = jnp.where(jnp.any(held, axis=-1)[..., None], slot_norms, empty_norm).reshape(-1)
    shares = jnp.exp(logits - row_norms[:, None]).astype(jnp.bfloat16)
    own_rows = centroids[0].astype(jnp.float32)
    marker = (jnp.arange(128, dtype=jnp.int32) == 0).astype(jnp.bfloat16)
    widened = jnp.concatenate(
        [incoming, jnp.broadcast_to(marker[None, :], (incoming.shape[0], 128))], axis=1
    )
    n_high, n_low = lax.axis_size("zh"), lax.axis_size("zl")
    halves = shares.reshape(shares.shape[0], 2, -1)

    def half_sums(which):
        return lax.dot_general(
            halves[:, which], widened, (((0,), (0,)), ((), ())), preferred_element_type=jnp.float32
        )

    sent = lax.ppermute(half_sums(1), "core", [(0, 1), (1, 0)])
    paired = lax.optimization_barrier(half_sums(0)) + sent
    paired = paired.reshape(n_low, n_high, -1, paired.shape[-1]).transpose(1, 0, 2, 3)
    paired = paired.reshape(n_high * n_low, -1, paired.shape[-1])
    reduced = lax.psum_scatter(paired, ("zh", "zl"), scatter_dimension=0, tiled=True)[0]
    new_sums = reduced[:, :width]
    new_mass = reduced[:, width]
    fresh = (new_sums + prior_weight * own_rows) / (new_mass[:, None] + prior_weight)
    return fresh[None]


def solution(mesh):
    cores = 2
    low = 4
    high = mesh.shape["dp"] // cores // low
    split = Mesh(
        mesh.devices.reshape(high, low, cores, mesh.shape["cent"]),
        ("zh", "zl", "core", "cent"),
    )
    rows = ("zh", "zl", "core")
    in_specs = (
        P((*rows, "cent"), None),
        P((*rows, "cent"), None),
        P((*rows, "cent")),
        P("cent", rows, None),
    )
    out_specs = P("cent", rows, None)
    return jax.shard_map(
        per_device, mesh=split, in_specs=in_specs, out_specs=out_specs, check_vma=False
    )
```
